32 devices in a mesh: ckpt: 2 (over x), train: 4 (over z), tensor: 4 (over y, core).
Axes of the slice: x: 2, y: 2, z: 4, core: 2. Of those that a mesh axis runs over, the one named last changes fastest.
Arguments:
- hidden: bfloat16 [2, 2048, 28672], P('ckpt', 'train', 'tensor'), may hold values from -6 to 6
- out_grads: bfloat16 [2, 2048, 8192], P('ckpt', 'train', 'tensor'), may hold values from -6 to 6
- proj_in: bfloat16 [64, 28672], P(None, 'tensor'), may hold values from -0.03125 to 0.03125
- proj_out: bfloat16 [64, 8192], P(None, 'tensor'), may hold values from -0.0625 to 0.0625
- test_grads: bfloat16 [2, 64, 4096], P('ckpt', ('train', 'tensor')), may hold values from -6 to 6
- step_weights: int32 [2], P('ckpt'), may hold values from 1 to 4
Outputs:
- scores: float32 [16, 4, 16], P('train', None, 'tensor')
The draws below stay inside these ranges and needn't reach their ends.
All inputs are finite; a program needn't handle non-finite values.
Results may differ from the reference program's by a relative error of at most 0.0029.
Values may be sent and summed in bfloat16 or wider, within the bound.
No kernel may reach another device: no remote copies, remote signals or barrier semaphores. Data moves between devices by JAX's collectives and lax.ppermute only.
A program may use at most 64 MiB of HBM per device.

```python
import math
import jax
import jax.numpy as jnp
from jax import lax

D = 8192
FF = 28672
KIN = 64
KOUT = 64
SEQ = 128
K = 4096
CKPT = 2
TEST_DEV = 4
TRAIN_EX = 16
TOKENS = 2048
NTEST = 64
N_TRAIN = 4
N_TENSOR = 4


def steps_of(key, dims, shards, least, largest):
    gain = 1.0
    for dim, blocks in shards:
        draws = jax.random.uniform(jax.random.fold_in(jax.random.fold_in(key, 6), dim), (blocks,), jnp.float32, least / len(shards), largest / len(shards))
        gain = gain * jnp.repeat(jnp.exp(draws), dims[dim] // blocks).reshape((-1,) + (1,) * (len(dims) - 1 - dim))
    return gain


def bell_draw(key, shape, spread, most, cuts=(), dtype=jnp.bfloat16):
    entries = jax.random.normal(key, shape, jnp.float32) * spread
    if len(cuts) > 0:
        entries = steps_of(key, shape, cuts, -0.22, 0.18) * entries
    return jnp.clip(entries, min=-most, max=most).astype(dtype)


def setup_inputs(seed: int = 0) -> dict:
    splits = jax.random.split(jax.random.key(seed), 7)
    hidden = bell_draw(splits[0], (CKPT, TOKENS, FF), 1.0, 6.0, ((0, 2), (1, 4), (2, 4)))
    out_grads = bell_draw(splits[1], (CKPT, TOKENS, D), 1.0, 6.0, ((0, 2), (1, 4), (2, 4)))
    proj_in = bell_draw(splits[2], (KIN, FF), FF ** -0.5, 0.03125, ((1, 4),))
    proj_out = bell_draw(splits[3], (KOUT, D), D ** -0.5, 0.0625, ((1, 4),))
    test_grads = bell_draw(splits[4], (CKPT, NTEST, K), 1.0, 6.0, ((0, 2), (1, 16)))
    step_weights = jax.random.randint(splits[5], (CKPT,), 1, 5).astype(jnp.int32)
    return dict(hidden=hidden, out_grads=out_grads, proj_in=proj_in, proj_out=proj_out, test_grads=test_grads, step_weights=step_weights)


def project_example(hidden_c, grads_c, proj_in, proj_out):
    left = jnp.dot(hidden_c, proj_in.T, preferred_element_type=jnp.float32)
    right = jnp.dot(grads_c, proj_out.T, preferred_element_type=jnp.float32)
    left = left.reshape(-1, SEQ, KIN)
    right = right.reshape(-1, SEQ, KOUT)
    outer = jnp.einsum('sto,sti->soi', right, left, precision=lax.Precision.HIGHEST)
    return outer.reshape(-1, KIN * KOUT).astype(jnp.bfloat16)

def reference(hidden, out_grads, proj_in, proj_out, test_grads, step_weights):
    scale = 1.0 / math.sqrt(SEQ * KIN * KOUT)
    total = jnp.zeros((TRAIN_EX, NTEST), jnp.float32)
    for index in range(CKPT):
        train = project_example(hidden[index], out_grads[index], proj_in, proj_out)
        raw = jnp.dot(train, test_grads[index].T, preferred_element_type=jnp.float32)
        weight = step_weights[index].astype(jnp.float32) * scale
        total = total + raw * weight
    return total.reshape(TRAIN_EX, N_TRAIN, N_TENSOR * TEST_DEV)
```

```python
import math

import jax
import jax.numpy as jnp
from jax import lax
from jax.sharding import PartitionSpec as P

KIN = 64
KOUT = 64
SEQ = 128


def outer_grads(sides):
    blocks = sides.reshape(-1, SEQ, KIN + KOUT)
    left = blocks[:, :, :KIN]
    right = blocks[:, :, KIN:]
    outer = jnp.einsum("sto,sti->soi", right, left, precision=lax.Precision.HIGHEST)
    return outer.reshape(-1, KIN * KOUT).astype(jnp.bfloat16)


def from_shift(x, axis, n, s):
    return lax.ppermute(x, axis, [((i + s) % n, i) for i in range(n)])


def gather(x, axis):
    n = lax.axis_size(axis)
    me = lax.axis_index(axis)
    pieces = jnp.stack([x] + [from_shift(x, axis, n, s) for s in range(1, n)])
    twice = jnp.concatenate([pieces, pieces])
    return lax.dynamic_slice_in_dim(twice, (n - me) % n, n, axis=0)


def reduce_scatter(x, axis):
    n = lax.axis_size(axis)
    me = lax.axis_index(axis)
    total = lax.dynamic_index_in_dim(x, me, axis=0, keepdims=False)
    for s in range(1, n):
        block = lax.dynamic_index_in_dim(x, (me + n - s) % n, axis=0, keepdims=False)
        total = total + from_shift(block, axis, n, s)
    return total


def body(hidden, out_grads, proj_in, proj_out, test_grads, step_weights):
    n_tensor = lax.axis_size("tensor")
    n_train = lax.axis_size("train")
    tests = gather(test_grads[0], "train")
    tests = tests.reshape(-1, tests.shape[-1])
    contract = (((1,), (1,)), ((), ()))
    left = lax.dot_general(hidden[0], proj_in, contract, preferred_element_type=jnp.float32)
    right = lax.dot_general(out_grads[0], proj_out, contract, preferred_element_type=jnp.float32)
    sides = jnp.concatenate([left, right], axis=1)
    sides = sides.reshape(n_tensor, -1, sides.shape[-1])
    own = outer_grads(reduce_scatter(sides, "tensor"))
    train_block = gather(own, "tensor").reshape(-1, own.shape[-1])
    table = lax.dot_general(train_block, tests, contract, preferred_element_type=jnp.float32)
    scale = 1.0 / math.sqrt(SEQ * KIN * KOUT)
    weight = step_weights[0].astype(jnp.float32) * scale
    terms = gather(table * weight, "ckpt")
    total = terms[0]
    for c in range(1, terms.shape[0]):
        total = total + terms[c]
    return total.reshape(train_block.shape[0], n_train, -1)


def solution(mesh):
    placed = (
        P("ckpt", "train", "tensor"),
        P("ckpt", "train", "tensor"),
        P(None, "tensor"),
        P(None, "tensor"),
        P("ckpt", ("train", "tensor"), None),
        P("ckpt"),
    )
    return jax.shard_map(
        body, mesh=mesh, in_specs=placed, out_specs=P("train", None, "tensor"), check_vma=False
    )
```

```python
import math

import jax
import jax.numpy as jnp
from jax import lax
from jax.sharding import PartitionSpec as P

KIN = 64
KOUT = 64
SEQ = 128


def outer_grads(sides):
    blocks = sides.reshape(-1, SEQ, KIN + KOUT)
    left = blocks[:, :, :KIN]
    right = blocks[:, :, KIN:]
    outer = jnp.einsum("sto,sti->soi", right, left, precision=lax.Precision.HIGHEST)
    return outer.reshape(-1, KIN * KOUT).astype(jnp.bfloat16)


def swap(x, axis, mask):
    n = lax.axis_size(axis)
    return lax.ppermute(x, axis, [(i, i ^ mask) for i in range(n)])


def high(axis, mask):
    return (lax.axis_index(axis) & mask) != 0


def masks_of(axis, start=0):
    n = lax.axis_size(axis)
    return [1 << b for b in range(start, n.bit_length() - 1)]


def gather(x, axis, masks):
    for mask in masks:
        other = swap(x, axis, mask)
        x = jnp.where(high(axis, mask), jnp.concatenate([other, x]), jnp.concatenate([x, other]))
    return x


def body(hidden, out_grads, proj_in, proj_out, test_grads, step_weights):
    n_train = lax.axis_size("train")
    tests = gather(test_grads[0], "train", masks_of("train"))
    contract = (((1,), (1,)), ((), ()))
    left = lax.dot_general(hidden[0], proj_in, contract, preferred_element_type=jnp.float32)
    right = lax.dot_general(out_grads[0], proj_out, contract, preferred_element_type=jnp.float32)
    sides = jnp.concatenate([left, right], axis=1)
    halves = sides.reshape(2, -1, sides.shape[-1])
    upper = high("tensor", 1)
    kept = jnp.where(upper, halves[1], halves[0])
    sent = jnp.where(upper, halves[0], halves[1])
    part = kept + swap(sent, "tensor", 1)
    for mask in masks_of("tensor", 1):
        part = part + swap(part, "tensor", mask)
    own = outer_grads(part)
    train_block = gather(own, "tensor", [1])
    table = lax.dot_general(train_block, tests, contract, preferred_element_type=jnp.float32)
    scale = 1.0 / math.sqrt(SEQ * KIN * KOUT)
    total = table * (step_weights[0].astype(jnp.float32) * scale)
    for mask in masks_of("ckpt"):
        total = total + swap(total, "ckpt", mask)
    return total.reshape(train_block.shape[0], n_train, -1)


def solution(mesh):
    placed = (
        P("ckpt", "train", "tensor"),
        P("ckpt", "train", "tensor"),
        P(None, "tensor"),
        P(None, "tensor"),
        P("ckpt", ("train", "tensor"), None),
        P("ckpt"),
    )
    return jax.shard_map(
        body, mesh=mesh, in_specs=placed, out_specs=P("train", None, "tensor"), check_vma=False
    )
```

```python
import math

import jax
import jax.numpy as jnp
from jax import lax
from jax.experimental import pallas as pl
from jax.experimental.pallas import tpu as pltpu
from jax.sharding import PartitionSpec as P

KIN = 64
KOUT = 64
SEQ = 128


def outer_grads(sides):
    blocks = sides.reshape(-1, SEQ, KIN + KOUT)
    left = blocks[:, :, :KIN]
    right = blocks[:, :, KIN:]
    outer = jnp.einsum("sto,sti->soi", right, left, precision=lax.Precision.HIGHEST)
    return outer.reshape(-1, KIN * KOUT).astype(jnp.bfloat16)


def project_kernel(upper_ref, lower_ref, proj_ref, out_ref, acc):
    step = pl.program_id(0)

    @pl.when(step == 0)
    def _():
        acc[...] = jnp.zeros_like(acc)

    rows = upper_ref.shape[0]
    contract = (((1,), (1,)), ((), ()))
    for j, ref in enumerate((upper_ref, lower_ref)):
        acc[:, j * rows:(j + 1) * rows] += lax.dot_general(
            proj_ref[...], ref[...], contract, preferred_element_type=jnp.float32
        )

    @pl.when(step == pl.num_programs(0) - 1)
    def _():
        out_ref[...] = acc[...]


def project_t(x, proj):
    rows, depth = x.shape
    width = proj.shape[0]
    chunk = depth // 2 if depth % 256 == 0 else depth
    half = rows // 2
    return pl.pallas_call(
        project_kernel,
        out_shape=jax.ShapeDtypeStruct((width, rows), jnp.float32),
        grid=(depth // chunk,),
        in_specs=[
            pl.BlockSpec((half, chunk), lambda k: (0, k)),
            pl.BlockSpec((half, chunk), lambda k: (1, k)),
            pl.BlockSpec((width, chunk), lambda k: (0, k)),
        ],
        out_specs=pl.BlockSpec((width, rows), lambda k: (0, 0)),
        scratch_shapes=[pltpu.VMEM((width, rows), jnp.float32)],
        compiler_params=pltpu.CompilerParams(dimension_semantics=("arbitrary",)),
        cost_estimate=pl.CostEstimate(
            flops=2 * rows * depth * width,
            bytes_accessed=2 * rows * depth + 2 * width * depth + 4 * width * rows,
            transcendentals=0,
        ),
    )(x, x, proj)


def swap(x, axis, mask):
    n = lax.axis_size(axis)
    return lax.ppermute(x, axis, [(i, i ^ mask) for i in range(n)])


def high(axis, mask):
    return (lax.axis_index(axis) & mask) != 0


def masks_of(axis, start=0):
    n = lax.axis_size(axis)
    return [1 << b for b in range(start, n.bit_length() - 1)]


def gather(x, axis, masks):
    for mask in masks:
        other = swap(x, axis, mask)
        x = jnp.where(high(axis, mask), jnp.concatenate([other, x]), jnp.concatenate([x, other]))
    return x


def body(hidden, out_grads, proj_in, proj_out, test_grads, step_weights):
    n_train = lax.axis_size("train")
    tests = gather(test_grads[0], "train", masks_of("train"))
    contract = (((1,), (1,)), ((), ()))
    left = project_t(hidden[0], proj_in).T
    right = lax.dot_general(out_grads[0], proj_out, contract, preferred_element_type=jnp.float32)
    sides = jnp.concatenate([left, right], axis=1)
    halves = sides.reshape(2, -1, sides.shape[-1])
    upper = high("tensor", 1)
    kept = jnp.where(upper, halves[1], halves[0])
    sent = jnp.where(upper, halves[0], halves[1])
    part = kept + swap(sent, "tensor", 1)
    for mask in masks_of("tensor", 1):
        part = part + swap(part, "tensor", mask)
    own = outer_grads(part)
    train_block = gather(own, "tensor", [1])
    table = lax.dot_general(train_block, tests, contract, preferred_element_type=jnp.float32)
    scale = 1.0 / math.sqrt(SEQ * KIN * KOUT)
    total = table * (step_weights[0].astype(jnp.float32) * scale)
    for mask in masks_of("ckpt"):
        total = total + swap(total, "ckpt", mask)
    return total.reshape(train_block.shape[0], n_train, -1)


def solution(mesh):
    placed = (
        P("ckpt", "train", "tensor"),
        P("ckpt", "train", "tensor"),
        P(None, "tensor"),
        P(None, "tensor"),
        P("ckpt", ("train", "tensor"), None),
        P("ckpt"),
    )
    return jax.shard_map(
        body, mesh=mesh, in_specs=placed, out_specs=P("train", None, "tensor"), check_vma=False
    )
```
